256 devices in a mesh: keys: 32 (over x, y, core), vocab: 8 (over z).
Axes of the slice: x: 4, y: 4, z: 8, core: 2. Of those that a mesh axis runs over, the one named last changes fastest.
Arguments:
- hidden: bfloat16 [1024, 4096], P(('keys', 'vocab')), may hold values from -24 to 24
- queries: bfloat16 [1024, 1024], P(('keys', 'vocab')), may hold values from -24 to 24
- probes: int32 [1024, 64], P(('keys', 'vocab')), may hold values from 0 to 95, as said below
- counts: int32 [1024], P(('keys', 'vocab')), may hold values from 16 to 64
- block_slot: int32 [96], replicated, may hold values from 0 to 95, as said below
- key_store: bfloat16 [96, 512, 1024], P('keys'), may hold values from -7 to 7
- stored_next_tokens: int32 [96, 512], replicated, may hold values from 0 to 128255
- head_weight: bfloat16 [4096, 128256], P(None, ('keys', 'vocab'))
Outputs:
- mixed_logp: float32 [1024, 128256], P(('keys', 'vocab'))
The draws below stay inside these ranges and needn't reach their ends.
Inputs may be any that keep to these rules, and one draw needn't show every extreme that they name: `probes`: the 64 ids of a row are distinct block ids; only the first counts of them are probed. At most 2 of a row's 64 ids map through block_slot to slots held by one keys index. `block_slot`: A permutation of the slots; slot s lies in the part of the key store held by keys index s // 3.
All inputs are finite; a program needn't handle non-finite values.
Results may differ from the reference program's by a relative error of at most 0.0003.
Values may be sent and summed in bfloat16 or wider, within the bound.
No kernel may reach another device: no remote copies, remote signals or barrier semaphores. Data moves between devices by JAX's collectives and lax.ppermute only.
A program may use at most 128 MiB of HBM per device.

```python
import math
import jax
import jax.numpy as jnp
import numpy as np
from jax import lax

D = 4096
VOCAB_ENTRIES = 128256
KEY_DIMENSION = 1024
KEYS_PER_BLOCK = 512
BLOCKS_PER_INDEX = 3
ROWS = 1024
TOTAL_BLOCKS = 96
PMAX = 64
PMIN = 16
OWN_MAX = 2


def slot_map(key):
    return jax.random.permutation(jax.random.fold_in(key, 13), TOTAL_BLOCKS).astype(jnp.int32)


def first_probes(row_random_key, inverse):
    owner_indices = TOTAL_BLOCKS // BLOCKS_PER_INDEX
    rank_positions = jax.random.permutation(jax.random.fold_in(row_random_key, 1), TOTAL_BLOCKS).astype(jnp.int32)
    inner = jnp.argsort(rank_positions.reshape(owner_indices, BLOCKS_PER_INDEX), axis=1, stable=True)[:, :OWN_MAX].astype(jnp.int32)
    slots = (jnp.arange(owner_indices, dtype=jnp.int32)[:, None] * BLOCKS_PER_INDEX + inner).reshape(owner_indices * OWN_MAX)
    order = jax.random.permutation(jax.random.fold_in(row_random_key, 2), owner_indices * OWN_MAX)[:PMAX]
    return inverse[slots[order]]


def probe_lists(key):
    row_keys = jax.random.split(jax.random.fold_in(key, 11), ROWS)
    inverse = jnp.argsort(slot_map(key), stable=True).astype(jnp.int32)
    return jax.vmap(first_probes, in_axes=(0, None))(row_keys, inverse).astype(jnp.int32)


def key_normals(key):
    return jnp.clip(jax.random.normal(jax.random.fold_in(key, 37), (TOTAL_BLOCKS, KEYS_PER_BLOCK, KEY_DIMENSION), jnp.float32), -6.0, 6.0)


def draw_probes(key, part):
    return probe_lists(key)


def draw_block_slot(key, part):
    return slot_map(key)


def draw_counts(key, part):
    base = jax.random.randint(jax.random.fold_in(key, 23), (ROWS,), PMIN, PMAX + 1, dtype=jnp.int32)
    first_row = jax.random.randint(jax.random.fold_in(key, 29), (), 0, ROWS, dtype=jnp.int32)
    offset = jax.random.randint(jax.random.fold_in(key, 31), (), 1, ROWS, dtype=jnp.int32)
    base = base.at[first_row].set(PMAX)
    return base.at[(first_row + offset) % ROWS].set(PMIN)


def draw_key_store(key, part):
    store = key_normals(key)
    return store.astype(jnp.bfloat16)


def draw_queries(key, part):
    normal_draw = jnp.clip(jax.random.normal(jax.random.fold_in(key, 53), (ROWS, KEY_DIMENSION), jnp.float32), -6.0, 6.0)
    return normal_draw.astype(jnp.bfloat16)


def draw_head_weight(key, part):
    weights = jnp.clip(jax.random.normal(jax.random.fold_in(key, 73), (D, VOCAB_ENTRIES), jnp.float32), -6.0, 6.0) * D ** (-0.5)
    fraction = jnp.arange(VOCAB_ENTRIES, dtype=jnp.float32) / VOCAB_ENTRIES
    ramp = 0.5 + 1.5 * fraction
    weights = weights * ramp[None, :]
    return weights.astype(jnp.bfloat16)


def draw_hidden(key, part):
    normal_draw = jnp.clip(jax.random.normal(jax.random.fold_in(key, 79), (ROWS, D), jnp.float32), -6.0, 6.0)
    return normal_draw.astype(jnp.bfloat16)


def with_ends(drawn, stream_key, least, largest):
    extent = drawn.shape
    place = [jax.random.randint(jax.random.fold_in(stream_key, axis), (), 0, extent[axis]) for axis in range(len(extent))]
    drawn = drawn.at[tuple(place)].set(least)
    longest = extent.index(max(extent))
    place[longest] = (place[longest] + 1) % extent[longest]
    return drawn.at[tuple(place)].set(largest)


def ranked_wide(key, dims, number_of, slope):
    weights = [min(1 << octave, number_of + 1 - (1 << octave)) * (1 << 20) // math.isqrt((1 << octave) ** slope) + 1 for octave in range((number_of + 1).bit_length()) if 1 << octave <= number_of]
    deviation = 1 + sum(weights) // (1 << 30)
    listing = np.cumsum(np.array([max(1, weight // deviation) for weight in weights]))
    lot = jax.random.randint(jax.random.fold_in(key, 1), dims, 0, int(listing[len(weights) - 1]))
    start = jnp.left_shift(1, jnp.searchsorted(jnp.asarray(listing, jnp.int32), lot, side="right").astype(jnp.int32))
    standing = start - 1 + jax.random.randint(jax.random.fold_in(key, 4), dims, 0, 1 << 30) % jnp.minimum(start, number_of + 1 - start)
    return jax.random.permutation(jax.random.fold_in(key, 2), number_of)[standing].astype(jnp.int32)


def setup_inputs(seed: int = 0) -> dict:
    seeds = jax.random.split(jax.random.key(seed), 9)
    hidden = draw_hidden(jax.random.fold_in(seeds[8], 71), 0)
    queries = draw_queries(jax.random.fold_in(seeds[8], 71), 0)
    probes = draw_probes(jax.random.fold_in(seeds[8], 71), 0)
    counts = draw_counts(jax.random.fold_in(seeds[8], 71), 0)
    block_slot = draw_block_slot(jax.random.fold_in(seeds[8], 71), 0)
    key_store = draw_key_store(jax.random.fold_in(seeds[8], 71), 0)
    stored_next_tokens = with_ends(ranked_wide(seeds[6], (TOTAL_BLOCKS, KEYS_PER_BLOCK), VOCAB_ENTRIES, 2), jax.random.fold_in(seeds[6], 3), 0, VOCAB_ENTRIES - 1).astype(jnp.int32)
    head_weight = draw_head_weight(jax.random.fold_in(seeds[8], 71), 0)
    return dict(hidden=hidden, queries=queries, probes=probes, counts=counts, block_slot=block_slot, key_store=key_store, stored_next_tokens=stored_next_tokens, head_weight=head_weight)


LAMBDA = 0.25
SMOOTH = 0.1

def pick_blocks(table, index_row):
    return table[index_row]

def reference(hidden, queries, probes, counts, block_slot, key_store, stored_next_tokens, head_weight):
    logits = jnp.dot(hidden, head_weight, preferred_element_type=jnp.float32)
    row_peak = lax.optimization_barrier(jnp.max(logits, axis=1, keepdims=True))
    log_probs = logits - (row_peak + jnp.log(lax.optimization_barrier(jnp.sum(jnp.exp(logits - row_peak), axis=1, keepdims=True))))
    key_width = key_store.shape[2]
    flat_keys = key_store.reshape(key_store.shape[0] * key_store.shape[1], key_width)
    key_norms = lax.optimization_barrier(jnp.sum(jnp.square(flat_keys.astype(jnp.float32)), axis=1))
    query_norms = lax.optimization_barrier(jnp.sum(jnp.square(queries.astype(jnp.float32)), axis=1))
    inner_prod = lax.dot_general(queries, flat_keys, (((1,), (1,)), ((), ())), preferred_element_type=jnp.float32)
    score_scale = 0.5 / math.sqrt(key_width)
    scores = -(query_norms[:, None] + key_norms[None, :] - 2.0 * inner_prod) * score_scale
    scores = scores.reshape(scores.shape[0], key_store.shape[0], key_store.shape[1])
    slot_ids = block_slot[probes]
    chosen = jax.vmap(pick_blocks)(scores, slot_ids)
    probe_cap = probes.shape[1]
    live_mask = (jnp.arange(probe_cap, dtype=jnp.int32)[None, :] < counts[:, None])[:, :, None]
    best_score = lax.optimization_barrier(jnp.max(jnp.where(live_mask, chosen, -jnp.inf), axis=(1, 2), keepdims=True))
    raised = jnp.where(live_mask, jnp.exp(chosen - best_score), 0.0)
    weights = raised / lax.optimization_barrier(jnp.sum(raised, axis=(1, 2), keepdims=True))
    tokens = stored_next_tokens[slot_ids]
    row_ids = jnp.broadcast_to(jnp.arange(tokens.shape[0], dtype=jnp.int32)[:, None, None], tokens.shape)
    vocab_size = logits.shape[1]
    knn_mass = jnp.zeros(logits.shape, jnp.float32).at[row_ids, tokens].add(weights)
    return jnp.log(LAMBDA * (knn_mass + SMOOTH / vocab_size) / (1.0 + SMOOTH) + (1.0 - LAMBDA) * jnp.exp(log_probs))
```

```python
import math

import jax
import jax.numpy as jnp
from jax import lax
from jax.experimental import pallas as pl
from jax.experimental.pallas import tpu as pltpu
from jax.sharding import PartitionSpec as P

LAMBDA = 0.25
SMOOTH = 0.1
LANES = 128


def code_range(vocab_size):
    floor = LAMBDA * (SMOOTH / vocab_size) / (1.0 + SMOOTH)
    return math.log(floor), math.log(floor + (1.0 - LAMBDA))


def knn_kernel(tok_ref, w_ref, out_ref, *accs):
    step = pl.program_id(0)

    @pl.when(step == 0)
    def _():
        for acc in accs:
            acc[...] = jnp.zeros_like(acc)

    lane = lax.broadcasted_iota(jnp.int32, (1, LANES), 1)

    def body(i, carry):
        for r, acc in enumerate(accs):
            token = tok_ref[r, i]
            weight = w_ref[r, i]
            row = token >> 7
            acc[pl.ds(row, 1), :] = acc[pl.ds(row, 1), :] + jnp.where(lane == (token & 127), weight, 0.0)
        return carry

    lax.fori_loop(0, tok_ref.shape[1], body, 0, unroll=8)

    @pl.when(step == pl.num_programs(0) - 1)
    def _():
        for r, acc in enumerate(accs):
            out_ref[r] = acc[...]


def knn_scatter(tokens, weights, vocab_size):
    rows, probes, block_len = tokens.shape
    tok = tokens.reshape(rows, probes * block_len)
    w = weights.reshape(rows, probes * block_len)
    lane_rows = vocab_size // LANES
    out = pl.pallas_call(
        knn_kernel,
        grid=(probes,),
        in_specs=[
            pl.BlockSpec((rows, block_len), lambda j: (0, j), memory_space=pltpu.SMEM),
            pl.BlockSpec((rows, block_len), lambda j: (0, j), memory_space=pltpu.SMEM),
        ],
        out_specs=pl.BlockSpec((rows, lane_rows, LANES), lambda j: (0, 0, 0)),
        out_shape=jax.ShapeDtypeStruct((rows, lane_rows, LANES), jnp.float32),
        scratch_shapes=[pltpu.VMEM((lane_rows, LANES), jnp.float32) for _ in range(rows)],
    )(tok, w)
    return out.reshape(rows, vocab_size)


def shards(hidden, queries, probes, counts, block_slot, key_store, stored_next_tokens, head_weight):
    rows_dev = hidden.shape[0]
    piece_cols = head_weight.shape[1]
    local_blocks = key_store.shape[0]
    block_len = key_store.shape[1]
    key_width = key_store.shape[2]
    key_count = lax.axis_size("keys")
    vocab_count = lax.axis_size("vocab")
    devices = key_count * vocab_count
    probe_cap = probes.shape[1]
    vocab_size = devices * piece_cols
    both = ("keys", "vocab")

    logits = jnp.dot(
        lax.all_gather(hidden, both, axis=0, tiled=True),
        head_weight,
        preferred_element_type=jnp.float32,
    )
    local_peak = jnp.max(logits, axis=1)
    row_peak = lax.pmax(local_peak, both)
    row_sum = lax.psum(jnp.sum(jnp.exp(logits - row_peak[:, None]), axis=1), both)
    log_probs = logits - (row_peak + jnp.log(row_sum))[:, None]
    floor = LAMBDA * (SMOOTH / vocab_size) / (1.0 + SMOOTH)
    lo, hi = code_range(vocab_size)
    base = jnp.log(floor + (1.0 - LAMBDA) * jnp.exp(log_probs))
    scale = 65535.0 / (hi - lo)
    code = (jnp.round((base - lo) * scale) - 32768.0).astype(jnp.int16)
    sent = code.reshape(devices, rows_dev, piece_cols)
    got = lax.all_to_all(sent, both, split_axis=0, concat_axis=0, tiled=True)
    got = got.reshape(devices, rows_dev, piece_cols).transpose(1, 0, 2).reshape(rows_dev, vocab_size)
    base_rows = (got.astype(jnp.float32) + 32768.0) * (1.0 / scale) + lo

    group_queries = lax.all_gather(queries, "keys", axis=0, tiled=True)
    flat_keys = key_store.reshape(local_blocks * block_len, key_width)
    key_norms = jnp.sum(jnp.square(flat_keys.astype(jnp.float32)), axis=1)
    query_norms = jnp.sum(jnp.square(group_queries.astype(jnp.float32)), axis=1)
    inner_prod = lax.dot_general(
        group_queries, flat_keys, (((1,), (1,)), ((), ())), preferred_element_type=jnp.float32
    )
    score_scale = 0.5 / math.sqrt(key_width)
    scores = -(query_norms[:, None] + key_norms[None, :] - 2.0 * inner_prod) * score_scale
    slot_ids = block_slot[probes]
    outgoing = scores.reshape(key_count, rows_dev, local_blocks, block_len)
    incoming = lax.all_to_all(outgoing, "keys", split_axis=0, concat_axis=2, tiled=True)
    every_slot = incoming.reshape(rows_dev, key_count * local_blocks, block_len)
    chosen = jnp.take_along_axis(every_slot, slot_ids[:, :, None], axis=1)
    live_mask = (jnp.arange(probe_cap, dtype=jnp.int32)[None, :] < counts[:, None])[:, :, None]
    best_score = jnp.max(jnp.where(live_mask, chosen, -jnp.inf), axis=(1, 2), keepdims=True)
    raised = jnp.where(live_mask, jnp.exp(chosen - best_score), 0.0)
    weights = raised / jnp.sum(raised, axis=(1, 2), keepdims=True)
    tokens = stored_next_tokens[slot_ids]
    knn_mass = knn_scatter(tokens, weights, vocab_size)
    mixed = jnp.log(jnp.exp(base_rows) + (LAMBDA / (1.0 + SMOOTH)) * knn_mass)
    return jnp.where(knn_mass > 0.0, mixed, base_rows)


def solution(mesh):
    placed = (
        P(("keys", "vocab"), None),
        P(("keys", "vocab"), None),
        P(("keys", "vocab"), None),
        P(("keys", "vocab")),
        P(),
        P("keys", None, None),
        P(),
        P(None, ("keys", "vocab")),
    )
    return jax.shard_map(
        shards, mesh=mesh, in_specs=placed, out_specs=P(("keys", "vocab"), None), check_vma=False
    )
```

```python
import math

import jax
import jax.numpy as jnp
from jax import lax
from jax.experimental import pallas as pl
from jax.experimental.pallas import tpu as pltpu
from jax.sharding import PartitionSpec as P

LAMBDA = 0.25
SMOOTH = 0.1
LANES = 128
CODE_DEPTH = 32.0


def knn_kernel(tok_ref, w_ref, out_ref, *accs):
    step = pl.program_id(0)

    @pl.when(step == 0)
    def _():
        for acc in accs:
            acc[...] = jnp.zeros_like(acc)

    lane = lax.broadcasted_iota(jnp.int32, (1, LANES), 1)

    def body(i, carry):
        for r, acc in enumerate(accs):
            token = tok_ref[r, i]
            weight = w_ref[r, i]
            row = token >> 7
            acc[pl.ds(row, 1), :] = acc[pl.ds(row, 1), :] + jnp.where(lane == (token & 127), weight, 0.0)
        return carry

    lax.fori_loop(0, tok_ref.shape[1], body, 0, unroll=8)

    @pl.when(step == pl.num_programs(0) - 1)
    def _():
        for r, acc in enumerate(accs):
            out_ref[r] = acc[...]


def knn_scatter(tokens, weights, vocab_size):
    rows, probes, block_len = tokens.shape
    tok = tokens.reshape(rows, probes * block_len)
    w = weights.reshape(rows, probes * block_len)
    lane_rows = vocab_size // LANES
    out = pl.pallas_call(
        knn_kernel,
        grid=(probes,),
        in_specs=[
            pl.BlockSpec((rows, block_len), lambda j: (0, j), memory_space=pltpu.SMEM),
            pl.BlockSpec((rows, block_len), lambda j: (0, j), memory_space=pltpu.SMEM),
        ],
        out_specs=pl.BlockSpec((rows, lane_rows, LANES), lambda j: (0, 0, 0)),
        out_shape=jax.ShapeDtypeStruct((rows, lane_rows, LANES), jnp.float32),
        scratch_shapes=[pltpu.VMEM((lane_rows, LANES), jnp.float32) for _ in range(rows)],
        cost_estimate=pl.CostEstimate(
            flops=4 * rows * probes * block_len * LANES,
            transcendentals=0,
            bytes_accessed=rows * probes * block_len * LANES * 8,
        ),
    )(tok, w)
    return out.reshape(rows, vocab_size)


def shards(hidden, queries, probes, counts, block_slot, key_store, stored_next_tokens, head_weight):
    rows_dev = hidden.shape[0]
    piece_cols = head_weight.shape[1]
    local_blocks = key_store.shape[0]
    block_len = key_store.shape[1]
    key_width = key_store.shape[2]
    key_count = lax.axis_size("keys")
    vocab_count = lax.axis_size("vocab")
    devices = key_count * vocab_count
    probe_cap = probes.shape[1]
    vocab_size = devices * piece_cols
    both = ("keys", "vocab")

    logits = jnp.dot(
        lax.all_gather(hidden, both, axis=0, tiled=True),
        head_weight,
        preferred_element_type=jnp.float32,
    )
    local_peak = jnp.max(logits, axis=1, keepdims=True)
    shifted = logits - local_peak
    local_sum = jnp.sum(jnp.exp(shifted), axis=1, keepdims=True)
    scale = 65535.0 / CODE_DEPTH
    code = (jnp.round((jnp.maximum(shifted, -CODE_DEPTH) + CODE_DEPTH) * scale) - 32768.0).astype(jnp.int16)
    got = lax.all_to_all(code.reshape(devices, rows_dev, piece_cols), both, split_axis=0, concat_axis=0, tiled=True)
    stats = jnp.concatenate([local_peak, local_sum], axis=1).reshape(devices, rows_dev, 2)
    got_stats = lax.all_to_all(stats, both, split_axis=0, concat_axis=0, tiled=True)
    got = got.reshape(devices, rows_dev, piece_cols)
    got_stats = got_stats.reshape(devices, rows_dev, 2)
    piece_peak = got_stats[:, :, 0]
    row_peak = jnp.max(piece_peak, axis=0)
    row_sum = jnp.sum(got_stats[:, :, 1] * jnp.exp(piece_peak - row_peak[None, :]), axis=0)
    offset = piece_peak - (row_peak + jnp.log(row_sum))[None, :]
    log_probs = (got.astype(jnp.float32) + 32768.0) * (1.0 / scale) - CODE_DEPTH + offset[:, :, None]
    log_probs = log_probs.transpose(1, 0, 2).reshape(rows_dev, vocab_size)

    group_queries = lax.all_gather(queries, "keys", axis=0, tiled=True)
    flat_keys = key_store.reshape(local_blocks * block_len, key_width)
    key_norms = jnp.sum(jnp.square(flat_keys.astype(jnp.float32)), axis=1)
    query_norms = jnp.sum(jnp.square(group_queries.astype(jnp.float32)), axis=1)
    inner_prod = lax.dot_general(
        group_queries, flat_keys, (((1,), (1,)), ((), ())), preferred_element_type=jnp.float32
    )
    score_scale = 0.5 / math.sqrt(key_width)
    scores = -(query_norms[:, None] + key_norms[None, :] - 2.0 * inner_prod) * score_scale
    slot_ids = block_slot[probes]
    outgoing = scores.reshape(key_count, rows_dev, local_blocks, block_len)
    incoming = lax.all_to_all(outgoing, "keys", split_axis=0, concat_axis=2, tiled=True)
    every_slot = incoming.reshape(rows_dev, key_count * local_blocks, block_len)
    chosen = jnp.take_along_axis(every_slot, slot_ids[:, :, None], axis=1)
    live_mask = (jnp.arange(probe_cap, dtype=jnp.int32)[None, :] < counts[:, None])[:, :, None]
    best_score = jnp.max(jnp.where(live_mask, chosen, -jnp.inf), axis=(1, 2), keepdims=True)
    raised = jnp.where(live_mask, jnp.exp(chosen - best_score), 0.0)
    weights = raised / jnp.sum(raised, axis=(1, 2), keepdims=True)
    tokens = stored_next_tokens[slot_ids]
    knn_mass = knn_scatter(tokens, weights, vocab_size)
    return jnp.log(
        LAMBDA * (knn_mass + SMOOTH / vocab_size) / (1.0 + SMOOTH)
        + (1.0 - LAMBDA) * jnp.exp(log_probs)
    )


def solution(mesh):
    placed = (
        P(("keys", "vocab"), None),
        P(("keys", "vocab"), None),
        P(("keys", "vocab"), None),
        P(("keys", "vocab")),
        P(),
        P("keys", None, None),
        P(),
        P(None, ("keys", "vocab")),
    )
    return jax.shard_map(
        shards, mesh=mesh, in_specs=placed, out_specs=P(("keys", "vocab"), None), check_vma=False
    )
```

```python
import math

import jax
import jax.numpy as jnp
from jax import lax
from jax.experimental import pallas as pl
from jax.experimental.pallas import tpu as pltpu
from jax.sharding import PartitionSpec as P

LAMBDA = 0.25
SMOOTH = 0.1
LANES = 128
CODE_DEPTH = 32.0


def knn_kernel(tok_ref, w_ref, init_ref, out_ref, *accs):
    step = pl.program_id(0)

    @pl.when(step == 0)
    def _():
        for r, acc in enumerate(accs):
            acc[...] = init_ref[r]

    lane = lax.broadcasted_iota(jnp.int32, (1, LANES), 1)

    def body(i, carry):
        for r, acc in enumerate(accs):
            token = tok_ref[r, i]
            weight = w_ref[r, i]
            row = token >> 7
            acc[pl.ds(row, 1), :] = acc[pl.ds(row, 1), :] + jnp.where(lane == (token & 127), weight, 0.0)
        return carry

    lax.fori_loop(0, tok_ref.shape[1], body, 0, unroll=8)

    @pl.when(step == pl.num_programs(0) - 1)
    def _():
        for r, acc in enumerate(accs):
            out_ref[r] = acc[...]


def knn_scatter(tokens, weights, init):
    rows, probes, block_len = tokens.shape
    tok = tokens.reshape(rows, probes * block_len)
    w = weights.reshape(rows, probes * block_len)
    lane_rows = init.shape[1]
    out = pl.pallas_call(
        knn_kernel,
        grid=(probes,),
        in_specs=[
            pl.BlockSpec((rows, block_len), lambda j: (0, j), memory_space=pltpu.SMEM),
            pl.BlockSpec((rows, block_len), lambda j: (0, j), memory_space=pltpu.SMEM),
            pl.BlockSpec((rows, lane_rows, LANES), lambda j: (0, 0, 0)),
        ],
        out_specs=pl.BlockSpec((rows, lane_rows, LANES), lambda j: (0, 0, 0)),
        out_shape=jax.ShapeDtypeStruct((rows, lane_rows, LANES), jnp.float32),
        scratch_shapes=[pltpu.VMEM((lane_rows, LANES), jnp.float32) for _ in range(rows)],
        cost_estimate=pl.CostEstimate(
            flops=4 * rows * probes * block_len * LANES,
            transcendentals=0,
            bytes_accessed=rows * probes * block_len * LANES * 8 + 8 * rows * lane_rows * LANES,
        ),
        input_output_aliases={2: 0},
    )(tok, w, init)
    return out


def shards(hidden, queries, probes, counts, block_slot, key_store, stored_next_tokens, head_weight):
    rows_dev = hidden.shape[0]
    piece_cols = head_weight.shape[1]
    local_blocks = key_store.shape[0]
    block_len = key_store.shape[1]
    key_width = key_store.shape[2]
    key_count = lax.axis_size("keys")
    vocab_count = lax.axis_size("vocab")
    devices = key_count * vocab_count
    probe_cap = probes.shape[1]
    vocab_size = devices * piece_cols
    both = ("keys", "vocab")

    group_queries = lax.all_gather(queries, "keys", axis=0, tiled=True)
    flat_keys = key_store.reshape(local_blocks * block_len, key_width)
    key_norms = jnp.sum(jnp.square(flat_keys.astype(jnp.float32)), axis=1)
    query_norms = jnp.sum(jnp.square(group_queries.astype(jnp.float32)), axis=1)
    inner_prod = lax.dot_general(
        group_queries, flat_keys, (((1,), (1,)), ((), ())), preferred_element_type=jnp.float32
    )
    score_scale = 0.5 / math.sqrt(key_width)
    scores = -(query_norms[:, None] + key_norms[None, :] - 2.0 * inner_prod) * score_scale
    slot_ids = block_slot[probes]
    outgoing = scores.reshape(key_count, rows_dev, local_blocks, block_len)
    incoming = lax.all_to_all(outgoing, "keys", split_axis=0, concat_axis=2, tiled=True)
    every_slot = incoming.reshape(rows_dev, key_count * local_blocks, block_len)
    chosen = jnp.take_along_axis(every_slot, slot_ids[:, :, None], axis=1)
    live_mask = (jnp.arange(probe_cap, dtype=jnp.int32)[None, :] < counts[:, None])[:, :, None]
    best_score = jnp.max(jnp.where(live_mask, chosen, -jnp.inf), axis=(1, 2), keepdims=True)
    raised = jnp.where(live_mask, jnp.exp(chosen - best_score), 0.0)
    weights = raised / jnp.sum(raised, axis=(1, 2), keepdims=True)
    tokens = stored_next_tokens[slot_ids]
    half = probe_cap // 2
    zeros = jnp.zeros((rows_dev, vocab_size // LANES, LANES), jnp.float32)
    knn_first = knn_scatter(tokens[:, :half], weights[:, :half], zeros)
    gathered = lax.all_gather(hidden, both, axis=0, tiled=False)
    gathered, knn_first = lax.optimization_barrier((gathered, knn_first))
    logits = jnp.einsum("dri,ic->drc", gathered, head_weight, preferred_element_type=jnp.float32)
    local_peak = jnp.max(logits, axis=2, keepdims=True)
    shifted = logits - local_peak
    local_sum = jnp.sum(jnp.exp(shifted), axis=2, keepdims=True)
    scale = 65535.0 / CODE_DEPTH
    code = (jnp.round((jnp.maximum(shifted, -CODE_DEPTH) + CODE_DEPTH) * scale) - 32768.0).astype(jnp.int16)
    stats = jnp.concatenate([local_peak, local_sum], axis=2)
    code, stats, knn_first = lax.optimization_barrier((code, stats, knn_first))
    got = lax.all_to_all(code, both, split_axis=0, concat_axis=0, tiled=True)
    got_stats = lax.all_to_all(stats, both, split_axis=0, concat_axis=0, tiled=True)
    knn_mass = knn_scatter(tokens[:, half:], weights[:, half:], knn_first).reshape(rows_dev, vocab_size)
    got = got.reshape(devices, rows_dev, piece_cols)
    got_stats = got_stats.reshape(devices, rows_dev, 2)
    piece_peak = got_stats[:, :, 0]
    row_peak = jnp.max(piece_peak, axis=0)
    row_sum = jnp.sum(got_stats[:, :, 1] * jnp.exp(piece_peak - row_peak[None, :]), axis=0)
    offset = piece_peak - (row_peak + jnp.log(row_sum))[None, :]
    log_probs = (got.astype(jnp.float32) + 32768.0) * (1.0 / scale) - CODE_DEPTH + offset[:, :, None]
    log_probs = log_probs.transpose(1, 0, 2).reshape(rows_dev, vocab_size)

    return jnp.log(
        LAMBDA * (knn_mass + SMOOTH / vocab_size) / (1.0 + SMOOTH)
        + (1.0 - LAMBDA) * jnp.exp(log_probs)
    )


def solution(mesh):
    placed = (
        P(("keys", "vocab"), None),
        P(("keys", "vocab"), None),
        P(("keys", "vocab"), None),
        P(("keys", "vocab")),
        P(),
        P("keys", None, None),
        P(),
        P(None, ("keys", "vocab")),
    )
    return jax.shard_map(
        shards, mesh=mesh, in_specs=placed, out_specs=P(("keys", "vocab"), None), check_vma=False
    )
```

```python
import math

import jax
import jax.numpy as jnp
from jax import lax
from jax.experimental import pallas as pl
from jax.experimental.pallas import tpu as pltpu
from jax.sharding import PartitionSpec as P

LAMBDA = 0.25
SMOOTH = 0.1
LANES = 128


def knn_kernel(tok_ref, w_ref, init_ref, out_ref, *accs):
    step = pl.program_id(0)

    @pl.when(step == 0)
    def _():
        for r, acc in enumerate(accs):
            acc[...] = init_ref[r]

    lane = lax.broadcasted_iota(jnp.int32, (1, LANES), 1)

    def body(i, carry):
        for r, acc in enumerate(accs):
            token = tok_ref[r, i]
            weight = w_ref[r, i]
            row = token >> 7
            acc[pl.ds(row, 1), :] = acc[pl.ds(row, 1), :] + jnp.where(lane == (token & 127), weight, 0.0)
        return carry

    lax.fori_loop(0, tok_ref.shape[1], body, 0, unroll=8)

    @pl.when(step == pl.num_programs(0) - 1)
    def _():
        for r, acc in enumerate(accs):
            out_ref[r] = acc[...]


def knn_scatter(tokens, weights, init):
    rows, probes, block_len = tokens.shape
    tok = tokens.reshape(rows, probes * block_len)
    w = weights.reshape(rows, probes * block_len)
    lane_rows = init.shape[1]
    out = pl.pallas_call(
        knn_kernel,
        grid=(probes,),
        in_specs=[
            pl.BlockSpec((rows, block_len), lambda j: (0, j), memory_space=pltpu.SMEM),
            pl.BlockSpec((rows, block_len), lambda j: (0, j), memory_space=pltpu.SMEM),
            pl.BlockSpec((rows, lane_rows, LANES), lambda j: (0, 0, 0)),
        ],
        out_specs=pl.BlockSpec((rows, lane_rows, LANES), lambda j: (0, 0, 0)),
        out_shape=jax.ShapeDtypeStruct((rows, lane_rows, LANES), jnp.float32),
        scratch_shapes=[pltpu.VMEM((lane_rows, LANES), jnp.float32) for _ in range(rows)],
        cost_estimate=pl.CostEstimate(
            flops=4 * rows * probes * block_len * LANES,
            transcendentals=0,
            bytes_accessed=rows * probes * block_len * LANES * 8 + 8 * rows * lane_rows * LANES,
        ),
        input_output_aliases={2: 0},
    )(tok, w, init)
    return out


def shards(hidden, queries, probes, counts, block_slot, key_store, stored_next_tokens, head_weight):
    rows_dev = hidden.shape[0]
    piece_cols = head_weight.shape[1]
    local_blocks = key_store.shape[0]
    block_len = key_store.shape[1]
    key_width = key_store.shape[2]
    key_count = lax.axis_size("keys")
    vocab_count = lax.axis_size("vocab")
    devices = key_count * vocab_count
    probe_cap = probes.shape[1]
    vocab_size = devices * piece_cols
    both = ("keys", "vocab")

    group_queries = lax.all_gather(queries, "keys", axis=0, tiled=True)
    flat_keys = key_store.reshape(local_blocks * block_len, key_width)
    key_norms = jnp.sum(jnp.square(flat_keys.astype(jnp.float32)), axis=1)
    query_norms = jnp.sum(jnp.square(group_queries.astype(jnp.float32)), axis=1)
    inner_prod = lax.dot_general(
        group_queries, flat_keys, (((1,), (1,)), ((), ())), preferred_element_type=jnp.float32
    )
    score_scale = 0.5 / math.sqrt(key_width)
    scores = -(query_norms[:, None] + key_norms[None, :] - 2.0 * inner_prod) * score_scale
    slot_ids = block_slot[probes]
    outgoing = scores.reshape(key_count, rows_dev, local_blocks, block_len)
    incoming = lax.all_to_all(outgoing, "keys", split_axis=0, concat_axis=2, tiled=True)
    every_slot = incoming.reshape(rows_dev, key_count * local_blocks, block_len)
    chosen = jnp.take_along_axis(every_slot, slot_ids[:, :, None], axis=1)
    live_mask = (jnp.arange(probe_cap, dtype=jnp.int32)[None, :] < counts[:, None])[:, :, None]
    best_score = jnp.max(jnp.where(live_mask, chosen, -jnp.inf), axis=(1, 2), keepdims=True)
    raised = jnp.where(live_mask, jnp.exp(chosen - best_score), 0.0)
    weights = raised / jnp.sum(raised, axis=(1, 2), keepdims=True)
    tokens = stored_next_tokens[slot_ids]
    half = probe_cap // 2
    zeros = jnp.zeros((rows_dev, vocab_size // LANES, LANES), jnp.float32)
    knn_first = knn_scatter(tokens[:, :half], weights[:, :half], zeros)
    gathered = lax.all_gather(hidden, both, axis=0, tiled=False)
    gathered, knn_first = lax.optimization_barrier((gathered, knn_first))
    logits = jnp.einsum("dri,ic->drc", gathered, head_weight, preferred_element_type=jnp.float32)
    local_peak = jnp.max(logits, axis=2, keepdims=True)
    shifted = logits - local_peak
    local_sum = jnp.sum(jnp.exp(shifted), axis=2, keepdims=True)
    payload = jnp.concatenate([shifted, local_peak, local_sum], axis=2)
    payload, knn_first = lax.optimization_barrier((payload, knn_first))
    got = lax.all_to_all(payload, both, split_axis=0, concat_axis=0, tiled=True)
    knn_mass = knn_scatter(tokens[:, half:], weights[:, half:], knn_first).reshape(rows_dev, vocab_size)
    got = got.reshape(devices, rows_dev, piece_cols + 2)
    piece_peak = got[:, :, piece_cols]
    row_peak = jnp.max(piece_peak, axis=0)
    row_sum = jnp.sum(got[:, :, piece_cols + 1] * jnp.exp(piece_peak - row_peak[None, :]), axis=0)
    offset = piece_peak - (row_peak + jnp.log(row_sum))[None, :]
    log_probs = got[:, :, :piece_cols] + offset[:, :, None]
    log_probs = log_probs.transpose(1, 0, 2).reshape(rows_dev, vocab_size)

    return jnp.log(
        LAMBDA * (knn_mass + SMOOTH / vocab_size) / (1.0 + SMOOTH)
        + (1.0 - LAMBDA) * jnp.exp(log_probs)
    )


def solution(mesh):
    placed = (
        P(("keys", "vocab"), None),
        P(("keys", "vocab"), None),
        P(("keys", "vocab"), None),
        P(("keys", "vocab")),
        P(),
        P("keys", None, None),
        P(),
        P(None, ("keys", "vocab")),
    )
    return jax.shard_map(
        shards, mesh=mesh, in_specs=placed, out_specs=P(("keys", "vocab"), None), check_vma=False
    )
```

```python
import functools
import math

import jax
import jax.numpy as jnp
from jax import lax
from jax.experimental import pallas as pl
from jax.experimental.pallas import tpu as pltpu
from jax.sharding import PartitionSpec as P

LAMBDA = 0.25
SMOOTH = 0.1
LANES = 128


def knn_kernel(base, rows_ref, steps_ref, tok_ref, w_ref, init_ref, out_ref, *accs):
    step = pl.program_id(0)
    rows = init_ref.shape[0]

    @pl.when(step == 0)
    def _():
        accs[0][...] = init_ref[...]
        for acc in accs[1:]:
            acc[...] = jnp.zeros_like(acc)

    lane = lax.broadcasted_iota(jnp.int32, (1, LANES), 1)
    pair = (base + step) * len(accs)

    @pl.when(base + step < steps_ref[0])
    def _():
        def body(i, carry):
            for k, acc in enumerate(accs):
                row = rows_ref[pair + k]
                token = tok_ref[k, i]
                weight = w_ref[k, i]
                line = token >> 7
                acc[row, pl.ds(line, 1), :] = acc[row, pl.ds(line, 1), :] + jnp.where(
                    lane == (token & 127), weight, 0.0
                )
            return carry

        lax.fori_loop(0, tok_ref.shape[1], body, 0, unroll=8)

    @pl.when(step == pl.num_programs(0) - 1)
    def _():
        for r in range(rows):
            total = accs[0][r]
            for acc in accs[1:]:
                total = total + acc[r]
            out_ref[r] = total


def knn_scatter(base, steps, pair_rows, tokens, weights, init):
    ways, probes, block_len = tokens.shape
    tok = tokens.reshape(ways, probes * block_len)
    w = weights.reshape(ways, probes * block_len)
    rows, lane_rows = init.shape[0], init.shape[1]
    return pl.pallas_call(
        functools.partial(knn_kernel, base),
        grid_spec=pltpu.PrefetchScalarGridSpec(
            num_scalar_prefetch=2,
            grid=(probes,),
            in_specs=[
                pl.BlockSpec((ways, block_len), lambda j, pr, st: (0, j), memory_space=pltpu.SMEM),
                pl.BlockSpec((ways, block_len), lambda j, pr, st: (0, j), memory_space=pltpu.SMEM),
                pl.BlockSpec((rows, lane_rows, LANES), lambda j, pr, st: (0, 0, 0)),
            ],
            out_specs=pl.BlockSpec((rows, lane_rows, LANES), lambda j, pr, st: (0, 0, 0)),
            scratch_shapes=[pltpu.VMEM((rows, lane_rows, LANES), jnp.float32) for _ in range(ways)],
        ),
        out_shape=jax.ShapeDtypeStruct((rows, lane_rows, LANES), jnp.float32),
        cost_estimate=pl.CostEstimate(
            flops=4 * ways * probes * block_len * LANES,
            transcendentals=0,
            bytes_accessed=ways * probes * block_len * LANES * 8 + 8 * rows * lane_rows * LANES,
        ),
        input_output_aliases={4: 0},
    )(pair_rows, steps, tok, w, init)


def shards(hidden, queries, probes, counts, block_slot, key_store, stored_next_tokens, head_weight):
    rows_dev = hidden.shape[0]
    piece_cols = head_weight.shape[1]
    local_blocks = key_store.shape[0]
    block_len = key_store.shape[1]
    key_width = key_store.shape[2]
    key_count = lax.axis_size("keys")
    vocab_count = lax.axis_size("vocab")
    devices = key_count * vocab_count
    probe_cap = probes.shape[1]
    vocab_size = devices * piece_cols
    both = ("keys", "vocab")

    group_queries = lax.all_gather(queries, "keys", axis=0, tiled=True)
    flat_keys = key_store.reshape(local_blocks * block_len, key_width)
    key_norms = jnp.sum(jnp.square(flat_keys.astype(jnp.float32)), axis=1)
    query_norms = jnp.sum(jnp.square(group_queries.astype(jnp.float32)), axis=1)
    inner_prod = lax.dot_general(
        group_queries, flat_keys, (((1,), (1,)), ((), ())), preferred_element_type=jnp.float32
    )
    score_scale = 0.5 / math.sqrt(key_width)
    scores = -(query_norms[:, None] + key_norms[None, :] - 2.0 * inner_prod) * score_scale
    slot_ids = block_slot[probes]
    outgoing = scores.reshape(key_count, rows_dev, local_blocks, block_len)
    incoming = lax.all_to_all(outgoing, "keys", split_axis=0, concat_axis=2, tiled=True)
    every_slot = incoming.reshape(rows_dev, key_count * local_blocks, block_len)
    chosen = jnp.take_along_axis(every_slot, slot_ids[:, :, None], axis=1)
    live_mask = (jnp.arange(probe_cap, dtype=jnp.int32)[None, :] < counts[:, None])[:, :, None]
    best_score = jnp.max(jnp.where(live_mask, chosen, -jnp.inf), axis=(1, 2), keepdims=True)
    raised = jnp.where(live_mask, jnp.exp(chosen - best_score), 0.0)
    weights = raised / jnp.sum(raised, axis=(1, 2), keepdims=True)
    tokens = stored_next_tokens[slot_ids]
    ways = rows_dev
    live_pairs = live_mask[:, :, 0].T.reshape(probe_cap * rows_dev)
    order = jnp.argsort(jnp.logical_not(live_pairs).astype(jnp.int32), stable=True).astype(jnp.int32)
    pair_rows = order % rows_dev
    pair_probes = order // rows_dev
    steps = ((jnp.sum(live_pairs.astype(jnp.int32)) + ways - 1) // ways).reshape(1)
    steps_total = probe_cap * rows_dev // ways
    tokens = tokens[pair_rows, pair_probes].reshape(steps_total, ways, block_len).transpose(1, 0, 2)
    weights = weights[pair_rows, pair_probes].reshape(steps_total, ways, block_len).transpose(1, 0, 2)
    half = steps_total // 2
    zeros = jnp.zeros((rows_dev, vocab_size // LANES, LANES), jnp.float32)
    knn_first = knn_scatter(0, steps, pair_rows, tokens[:, :half], weights[:, :half], zeros)
    gathered = lax.all_gather(hidden, both, axis=0, tiled=False)
    gathered, knn_first = lax.optimization_barrier((gathered, knn_first))
    logits = jnp.einsum("dri,ic->drc", gathered, head_weight, preferred_element_type=jnp.float32)
    local_peak = jnp.max(logits, axis=2, keepdims=True)
    shifted = logits - local_peak
    local_sum = jnp.sum(jnp.exp(shifted), axis=2, keepdims=True)
    payload = jnp.concatenate([shifted, local_peak, local_sum], axis=2)
    payload, knn_first = lax.optimization_barrier((payload, knn_first))
    got = lax.all_to_all(payload, both, split_axis=0, concat_axis=0, tiled=True)
    knn_mass = knn_scatter(half, steps, pair_rows, tokens[:, half:], weights[:, half:], knn_first)
    knn_mass = knn_mass.reshape(rows_dev, vocab_size)
    got = got.reshape(devices, rows_dev, piece_cols + 2)
    piece_peak = got[:, :, piece_cols]
    row_peak = jnp.max(piece_peak, axis=0)
    row_sum = jnp.sum(got[:, :, piece_cols + 1] * jnp.exp(piece_peak - row_peak[None, :]), axis=0)
    offset = piece_peak - (row_peak + jnp.log(row_sum))[None, :]
    log_probs = got[:, :, :piece_cols] + offset[:, :, None]
    log_probs = log_probs.transpose(1, 0, 2).reshape(rows_dev, vocab_size)

    return jnp.log(
        LAMBDA * (knn_mass + SMOOTH / vocab_size) / (1.0 + SMOOTH)
        + (1.0 - LAMBDA) * jnp.exp(log_probs)
    )


def solution(mesh):
    placed = (
        P(("keys", "vocab"), None),
        P(("keys", "vocab"), None),
        P(("keys", "vocab"), None),
        P(("keys", "vocab")),
        P(),
        P("keys", None, None),
        P(),
        P(None, ("keys", "vocab")),
    )
    return jax.shard_map(
        shards, mesh=mesh, in_specs=placed, out_specs=P(("keys", "vocab"), None), check_vma=False
    )
```

```python
import math

import jax
import jax.numpy as jnp
from jax import lax
from jax.experimental import pallas as pl
from jax.experimental.pallas import tpu as pltpu
from jax.sharding import PartitionSpec as P

LAMBDA = 0.25
SMOOTH = 0.1
LANES = 128


def knn_kernel(tok_ref, w_ref, init_ref, out_ref, *accs):
    step = pl.program_id(0)

    @pl.when(step == 0)
    def _():
        for r, acc in enumerate(accs):
            acc[...] = init_ref[r]

    lane = lax.broadcasted_iota(jnp.int32, (1, LANES), 1)

    def body(i, carry):
        for r, acc in enumerate(accs):
            token = tok_ref[r, i]
            weight = w_ref[r, i]
            row = token >> 7
            acc[pl.ds(row, 1), :] = acc[pl.ds(row, 1), :] + jnp.where(lane == (token & 127), weight, 0.0)
        return carry

    lax.fori_loop(0, tok_ref.shape[1], body, 0, unroll=32)

    @pl.when(step == pl.num_programs(0) - 1)
    def _():
        for r, acc in enumerate(accs):
            out_ref[r] = acc[...]


def knn_scatter(tokens, weights, init):
    rows, probes, block_len = tokens.shape
    tok = tokens.reshape(rows, probes * block_len)
    w = weights.reshape(rows, probes * block_len)
    lane_rows = init.shape[1]
    out = pl.pallas_call(
        knn_kernel,
        grid=(probes,),
        in_specs=[
            pl.BlockSpec((rows, block_len), lambda j: (0, j), memory_space=pltpu.SMEM),
            pl.BlockSpec((rows, block_len), lambda j: (0, j), memory_space=pltpu.SMEM),
            pl.BlockSpec((rows, lane_rows, LANES), lambda j: (0, 0, 0)),
        ],
        out_specs=pl.BlockSpec((rows, lane_rows, LANES), lambda j: (0, 0, 0)),
        out_shape=jax.ShapeDtypeStruct((rows, lane_rows, LANES), jnp.float32),
        scratch_shapes=[pltpu.VMEM((lane_rows, LANES), jnp.float32) for _ in range(rows)],
        cost_estimate=pl.CostEstimate(
            flops=4 * rows * probes * block_len * LANES,
            transcendentals=0,
            bytes_accessed=rows * probes * block_len * LANES * 8 + 8 * rows * lane_rows * LANES,
        ),
        input_output_aliases={2: 0},
    )(tok, w, init)
    return out


def shards(hidden, queries, probes, counts, block_slot, key_store, stored_next_tokens, head_weight):
    rows_dev = hidden.shape[0]
    piece_cols = head_weight.shape[1]
    local_blocks = key_store.shape[0]
    block_len = key_store.shape[1]
    key_width = key_store.shape[2]
    key_count = lax.axis_size("keys")
    vocab_count = lax.axis_size("vocab")
    devices = key_count * vocab_count
    probe_cap = probes.shape[1]
    vocab_size = devices * piece_cols
    both = ("keys", "vocab")

    group_queries = lax.all_gather(queries, "keys", axis=0, tiled=True)
    flat_keys = key_store.reshape(local_blocks * block_len, key_width)
    key_norms = jnp.sum(jnp.square(flat_keys.astype(jnp.float32)), axis=1)
    query_norms = jnp.sum(jnp.square(group_queries.astype(jnp.float32)), axis=1)
    inner_prod = lax.dot_general(
        group_queries, flat_keys, (((1,), (1,)), ((), ())), preferred_element_type=jnp.float32
    )
    score_scale = 0.5 / math.sqrt(key_width)
    scores = -(query_norms[:, None] + key_norms[None, :] - 2.0 * inner_prod) * score_scale
    slot_ids = block_slot[probes]
    outgoing = scores.reshape(key_count, rows_dev, local_blocks, block_len)
    incoming = lax.all_to_all(outgoing, "keys", split_axis=0, concat_axis=2, tiled=True)
    every_slot = incoming.reshape(rows_dev, key_count * local_blocks, block_len)
    chosen = jnp.take_along_axis(every_slot, slot_ids[:, :, None], axis=1)
    live_mask = (jnp.arange(probe_cap, dtype=jnp.int32)[None, :] < counts[:, None])[:, :, None]
    best_score = jnp.max(jnp.where(live_mask, chosen, -jnp.inf), axis=(1, 2), keepdims=True)
    raised = jnp.where(live_mask, jnp.exp(chosen - best_score), 0.0)
    weights = raised / jnp.sum(raised, axis=(1, 2), keepdims=True)
    tokens = stored_next_tokens[slot_ids]
    half = probe_cap // 2
    zeros = jnp.zeros((rows_dev, vocab_size // LANES, LANES), jnp.float32)
    knn_first = knn_scatter(tokens[:, :half], weights[:, :half], zeros)
    gathered = lax.all_gather(hidden, both, axis=0, tiled=False)
    gathered, knn_first = lax.optimization_barrier((gathered, knn_first))
    logits = jnp.einsum("dri,ic->drc", gathered, head_weight, preferred_element_type=jnp.float32)
    local_peak = jnp.max(logits, axis=2, keepdims=True)
    shifted = logits - local_peak
    local_sum = jnp.sum(jnp.exp(shifted), axis=2, keepdims=True)
    payload = jnp.concatenate([shifted, local_peak, local_sum], axis=2)
    payload, knn_first = lax.optimization_barrier((payload, knn_first))
    got = lax.all_to_all(payload, both, split_axis=0, concat_axis=0, tiled=True)
    knn_mass = knn_scatter(tokens[:, half:], weights[:, half:], knn_first).reshape(rows_dev, vocab_size)
    got = got.reshape(devices, rows_dev, piece_cols + 2)
    piece_peak = got[:, :, piece_cols]
    row_peak = jnp.max(piece_peak, axis=0)
    row_sum = jnp.sum(got[:, :, piece_cols + 1] * jnp.exp(piece_peak - row_peak[None, :]), axis=0)
    offset = piece_peak - (row_peak + jnp.log(row_sum))[None, :]
    log_probs = got[:, :, :piece_cols] + offset[:, :, None]
    log_probs = log_probs.transpose(1, 0, 2).reshape(rows_dev, vocab_size)

    return jnp.log(
        LAMBDA * (knn_mass + SMOOTH / vocab_size) / (1.0 + SMOOTH)
        + (1.0 - LAMBDA) * jnp.exp(log_probs)
    )


def solution(mesh):
    placed = (
        P(("keys", "vocab"), None),
        P(("keys", "vocab"), None),
        P(("keys", "vocab"), None),
        P(("keys", "vocab")),
        P(),
        P("keys", None, None),
        P(),
        P(None, ("keys", "vocab")),
    )
    return jax.shard_map(
        shards, mesh=mesh, in_specs=placed, out_specs=P(("keys", "vocab"), None), check_vma=False
    )
```

```python
import math

import jax
import jax.numpy as jnp
from jax import lax
from jax.experimental import pallas as pl
from jax.experimental.pallas import tpu as pltpu
from jax.sharding import PartitionSpec as P

LAMBDA = 0.25
SMOOTH = 0.1
LANES = 128


def knn_kernel(line_ref, lane_ref, w_ref, init_ref, out_ref, *accs):
    step = pl.program_id(0)

    @pl.when(step == 0)
    def _():
        for r, acc in enumerate(accs):
            acc[...] = init_ref[r]

    lane = lax.broadcasted_iota(jnp.int32, (1, LANES), 1)

    def body(i, carry):
        for r, acc in enumerate(accs):
            row = line_ref[r, i]
            place = lane_ref[r, i]
            weight = w_ref[r, i]
            acc[pl.ds(row, 1), :] = acc[pl.ds(row, 1), :] + jnp.where(lane == place, weight, 0.0)
        return carry

    lax.fori_loop(0, line_ref.shape[1], body, 0, unroll=32)

    @pl.when(step == pl.num_programs(0) - 1)
    def _():
        for r, acc in enumerate(accs):
            out_ref[r] = acc[...]


def knn_scatter(tokens, weights, init):
    rows, probes, block_len = tokens.shape
    tok = tokens.reshape(rows, probes * block_len)
    w = weights.reshape(rows, probes * block_len)
    lane_rows = init.shape[1]
    out = pl.pallas_call(
        knn_kernel,
        grid=(probes,),
        in_specs=[
            pl.BlockSpec((rows, block_len), lambda j: (0, j), memory_space=pltpu.SMEM),
            pl.BlockSpec((rows, block_len), lambda j: (0, j), memory_space=pltpu.SMEM),
            pl.BlockSpec((rows, block_len), lambda j: (0, j), memory_space=pltpu.SMEM),
            pl.BlockSpec((rows, lane_rows, LANES), lambda j: (0, 0, 0)),
        ],
        out_specs=pl.BlockSpec((rows, lane_rows, LANES), lambda j: (0, 0, 0)),
        out_shape=jax.ShapeDtypeStruct((rows, lane_rows, LANES), jnp.float32),
        scratch_shapes=[pltpu.VMEM((lane_rows, LANES), jnp.float32) for _ in range(rows)],
        cost_estimate=pl.CostEstimate(
            flops=4 * rows * probes * block_len * LANES,
            transcendentals=0,
            bytes_accessed=rows * probes * block_len * LANES * 8 + 8 * rows * lane_rows * LANES,
        ),
        input_output_aliases={3: 0},
    )(tok >> 7, tok & (LANES - 1), w, init)
    return out


def shards(hidden, queries, probes, counts, block_slot, key_store, stored_next_tokens, head_weight):
    rows_dev = hidden.shape[0]
    piece_cols = head_weight.shape[1]
    local_blocks = key_store.shape[0]
    block_len = key_store.shape[1]
    key_width = key_store.shape[2]
    key_count = lax.axis_size("keys")
    vocab_count = lax.axis_size("vocab")
    devices = key_count * vocab_count
    probe_cap = probes.shape[1]
    vocab_size = devices * piece_cols
    both = ("keys", "vocab")

    group_queries = lax.all_gather(queries, "keys", axis=0, tiled=True)
    flat_keys = key_store.reshape(local_blocks * block_len, key_width)
    key_norms = jnp.sum(jnp.square(flat_keys.astype(jnp.float32)), axis=1)
    query_norms = jnp.sum(jnp.square(group_queries.astype(jnp.float32)), axis=1)
    inner_prod = lax.dot_general(
        group_queries, flat_keys, (((1,), (1,)), ((), ())), preferred_element_type=jnp.float32
    )
    score_scale = 0.5 / math.sqrt(key_width)
    scores = -(query_norms[:, None] + key_norms[None, :] - 2.0 * inner_prod) * score_scale
    slot_ids = block_slot[probes]
    outgoing = scores.reshape(key_count, rows_dev, local_blocks, block_len)
    incoming = lax.all_to_all(outgoing, "keys", split_axis=0, concat_axis=2, tiled=True)
    every_slot = incoming.reshape(rows_dev, key_count * local_blocks, block_len)
    chosen = jnp.take_along_axis(every_slot, slot_ids[:, :, None], axis=1)
    live_mask = (jnp.arange(probe_cap, dtype=jnp.int32)[None, :] < counts[:, None])[:, :, None]
    best_score = jnp.max(jnp.where(live_mask, chosen, -jnp.inf), axis=(1, 2), keepdims=True)
    raised = jnp.where(live_mask, jnp.exp(chosen - best_score), 0.0)
    weights = raised / jnp.sum(raised, axis=(1, 2), keepdims=True)
    tokens = stored_next_tokens[slot_ids]
    half = probe_cap // 2
    zeros = jnp.zeros((rows_dev, vocab_size // LANES, LANES), jnp.float32)
    knn_first = knn_scatter(tokens[:, :half], weights[:, :half], zeros)
    gathered = lax.all_gather(hidden, both, axis=0, tiled=False)
    gathered, knn_first = lax.optimization_barrier((gathered, knn_first))
    logits = jnp.einsum("dri,ic->drc", gathered, head_weight, preferred_element_type=jnp.float32)
    local_peak = jnp.max(logits, axis=2, keepdims=True)
    shifted = logits - local_peak
    local_sum = jnp.sum(jnp.exp(shifted), axis=2, keepdims=True)
    payload = jnp.concatenate([shifted, local_peak, local_sum], axis=2)
    payload, knn_first = lax.optimization_barrier((payload, knn_first))
    got = lax.all_to_all(payload, both, split_axis=0, concat_axis=0, tiled=True)
    knn_mass = knn_scatter(tokens[:, half:], weights[:, half:], knn_first).reshape(rows_dev, vocab_size)
    got = got.reshape(devices, rows_dev, piece_cols + 2)
    piece_peak = got[:, :, piece_cols]
    row_peak = jnp.max(piece_peak, axis=0)
    row_sum = jnp.sum(got[:, :, piece_cols + 1] * jnp.exp(piece_peak - row_peak[None, :]), axis=0)
    offset = piece_peak - (row_peak + jnp.log(row_sum))[None, :]
    log_probs = got[:, :, :piece_cols] + offset[:, :, None]
    log_probs = log_probs.transpose(1, 0, 2).reshape(rows_dev, vocab_size)

    return jnp.log(
        LAMBDA * (knn_mass + SMOOTH / vocab_size) / (1.0 + SMOOTH)
        + (1.0 - LAMBDA) * jnp.exp(log_probs)
    )


def solution(mesh):
    placed = (
        P(("keys", "vocab"), None),
        P(("keys", "vocab"), None),
        P(("keys", "vocab"), None),
        P(("keys", "vocab")),
        P(),
        P("keys", None, None),
        P(),
        P(None, ("keys", "vocab")),
    )
    return jax.shard_map(
        shards, mesh=mesh, in_specs=placed, out_specs=P(("keys", "vocab"), None), check_vma=False
    )
```

```python
import math

import jax
import jax.numpy as jnp
from jax import lax
from jax.experimental import pallas as pl
from jax.experimental.pallas import tpu as pltpu
from jax.sharding import PartitionSpec as P

LAMBDA = 0.25
SMOOTH = 0.1
LANES = 128


def knn_kernel(line_ref, lane_ref, w_ref, init_ref, out_ref, *accs):
    step = pl.program_id(0)

    @pl.when(step == 0)
    def _():
        for r, acc in enumerate(accs):
            acc[...] = init_ref[r]

    lane = lax.broadcasted_iota(jnp.int32, (1, LANES), 1)

    def body(i, carry):
        for r, acc in enumerate(accs):
            row = line_ref[r, i]
            place = lane_ref[r, i]
            weight = w_ref[r, i]
            acc[pl.ds(row, 1), :] = acc[pl.ds(row, 1), :] + jnp.where(lane == place, weight, 0.0)
        return carry

    lax.fori_loop(0, line_ref.shape[1], body, 0, unroll=32)

    @pl.when(step == pl.num_programs(0) - 1)
    def _():
        for r, acc in enumerate(accs):
            out_ref[r] = acc[...]


def knn_scatter(tokens, weights, init):
    rows, probes, block_len = tokens.shape
    tok = tokens.reshape(rows, probes * block_len)
    w = weights.reshape(rows, probes * block_len)
    lane_rows = init.shape[1]
    out = pl.pallas_call(
        knn_kernel,
        grid=(probes,),
        in_specs=[
            pl.BlockSpec((rows, block_len), lambda j: (0, j), memory_space=pltpu.SMEM),
            pl.BlockSpec((rows, block_len), lambda j: (0, j), memory_space=pltpu.SMEM),
            pl.BlockSpec((rows, block_len), lambda j: (0, j), memory_space=pltpu.SMEM),
            pl.BlockSpec((rows, lane_rows, LANES), lambda j: (0, 0, 0)),
        ],
        out_specs=pl.BlockSpec((rows, lane_rows, LANES), lambda j: (0, 0, 0)),
        out_shape=jax.ShapeDtypeStruct((rows, lane_rows, LANES), jnp.float32),
        scratch_shapes=[pltpu.VMEM((lane_rows, LANES), jnp.float32) for _ in range(rows)],
        cost_estimate=pl.CostEstimate(
            flops=4 * rows * probes * block_len * LANES,
            transcendentals=0,
            bytes_accessed=rows * probes * block_len * LANES * 8 + 8 * rows * lane_rows * LANES,
        ),
        input_output_aliases={3: 0},
    )(tok >> 7, tok & (LANES - 1), w, init)
    return out


def shards(hidden, queries, probes, counts, block_slot, key_store, stored_next_tokens, head_weight):
    rows_dev = hidden.shape[0]
    piece_cols = head_weight.shape[1]
    local_blocks = key_store.shape[0]
    block_len = key_store.shape[1]
    key_width = key_store.shape[2]
    key_count = lax.axis_size("keys")
    vocab_count = lax.axis_size("vocab")
    devices = key_count * vocab_count
    probe_cap = probes.shape[1]
    vocab_size = devices * piece_cols
    both = ("keys", "vocab")

    group_queries = lax.all_gather(queries, "keys", axis=0, tiled=True)
    flat_keys = key_store.reshape(local_blocks * block_len, key_width)
    key_norms = jnp.sum(jnp.square(flat_keys.astype(jnp.float32)), axis=1)
    query_norms = jnp.sum(jnp.square(group_queries.astype(jnp.float32)), axis=1)
    inner_prod = lax.dot_general(
        group_queries, flat_keys, (((1,), (1,)), ((), ())), preferred_element_type=jnp.float32
    )
    score_scale = 0.5 / math.sqrt(key_width)
    scores = -(query_norms[:, None] + key_norms[None, :] - 2.0 * inner_prod) * score_scale
    slot_ids = block_slot[probes]
    outgoing = scores.reshape(key_count, rows_dev, local_blocks, block_len)
    incoming = lax.all_to_all(outgoing, "keys", split_axis=0, concat_axis=2, tiled=True)
    every_slot = incoming.reshape(rows_dev, key_count * local_blocks, block_len)
    chosen = jnp.take_along_axis(every_slot, slot_ids[:, :, None], axis=1)
    live_mask = (jnp.arange(probe_cap, dtype=jnp.int32)[None, :] < counts[:, None])[:, :, None]
    best_score = jnp.max(jnp.where(live_mask, chosen, -jnp.inf), axis=(1, 2), keepdims=True)
    raised = jnp.where(live_mask, jnp.exp(chosen - best_score), 0.0)
    weights = raised / jnp.sum(raised, axis=(1, 2), keepdims=True)
    tokens = stored_next_tokens[slot_ids]
    half = probe_cap // 2
    zeros = jnp.zeros((rows_dev, vocab_size // LANES, LANES), jnp.float32)
    knn_first = knn_scatter(tokens[:, :half], weights[:, :half], zeros)
    gathered = lax.all_gather(hidden, both, axis=0, tiled=False)
    gathered, knn_first = lax.optimization_barrier((gathered, knn_first))
    logits = jnp.einsum("dri,ic->drc", gathered, head_weight, preferred_element_type=jnp.float32)
    local_peak = jnp.max(logits, axis=2, keepdims=True)
    shifted = logits - local_peak
    local_sum = jnp.sum(jnp.exp(shifted), axis=2, keepdims=True)
    spare = jnp.zeros(shifted.shape[:2] + (LANES - (piece_cols + 2) % LANES,), jnp.float32)
    payload = jnp.concatenate([shifted, local_peak, local_sum, spare], axis=2)
    payload, knn_first = lax.optimization_barrier((payload, knn_first))
    got = lax.all_to_all(payload, both, split_axis=0, concat_axis=0, tiled=True)
    knn_mass = knn_scatter(tokens[:, half:], weights[:, half:], knn_first).reshape(rows_dev, vocab_size)
    got = got.reshape(devices, rows_dev, payload.shape[2])
    piece_peak = got[:, :, piece_cols]
    row_peak = jnp.max(piece_peak, axis=0)
    row_sum = jnp.sum(got[:, :, piece_cols + 1] * jnp.exp(piece_peak - row_peak[None, :]), axis=0)
    offset = piece_peak - (row_peak + jnp.log(row_sum))[None, :]
    log_probs = got[:, :, :piece_cols] + offset[:, :, None]
    log_probs = log_probs.transpose(1, 0, 2).reshape(rows_dev, vocab_size)

    return jnp.log(
        LAMBDA * (knn_mass + SMOOTH / vocab_size) / (1.0 + SMOOTH)
        + (1.0 - LAMBDA) * jnp.exp(log_probs)
    )


def solution(mesh):
    placed = (
        P(("keys", "vocab"), None),
        P(("keys", "vocab"), None),
        P(("keys", "vocab"), None),
        P(("keys", "vocab")),
        P(),
        P("keys", None, None),
        P(),
        P(None, ("keys", "vocab")),
    )
    return jax.shard_map(
        shards, mesh=mesh, in_specs=placed, out_specs=P(("keys", "vocab"), None), check_vma=False
    )
```

```python
import math

import jax
import jax.numpy as jnp
from jax import lax
from jax.experimental import pallas as pl
from jax.experimental.pallas import tpu as pltpu
from jax.sharding import PartitionSpec as P

LAMBDA = 0.25
SMOOTH = 0.1
LANES = 128


def knn_kernel(line_ref, lane_ref, w_ref, init_ref, out_ref, *accs):
    step = pl.program_id(0)

    @pl.when(step == 0)
    def _():
        for r, acc in enumerate(accs):
            acc[...] = init_ref[r]

    lane = lax.broadcasted_iota(jnp.int32, (1, LANES), 1)

    def body(i, carry):
        for r, acc in enumerate(accs):
            row = line_ref[r, i]
            place = lane_ref[r, i]
            weight = w_ref[r, i]
            acc[pl.ds(row, 1), :] = acc[pl.ds(row, 1), :] + jnp.where(lane == place, weight, 0.0)
        return carry

    lax.fori_loop(0, line_ref.shape[1], body, 0, unroll=64)

    @pl.when(step == pl.num_programs(0) - 1)
    def _():
        for r, acc in enumerate(accs):
            out_ref[r] = acc[...]


def knn_scatter(tokens, weights, init):
    rows, probes, block_len = tokens.shape
    tok = tokens.reshape(rows, probes * block_len)
    w = weights.reshape(rows, probes * block_len)
    lane_rows = init.shape[1]
    out = pl.pallas_call(
        knn_kernel,
        grid=(probes,),
        in_specs=[
            pl.BlockSpec((rows, block_len), lambda j: (0, j), memory_space=pltpu.SMEM),
            pl.BlockSpec((rows, block_len), lambda j: (0, j), memory_space=pltpu.SMEM),
            pl.BlockSpec((rows, block_len), lambda j: (0, j), memory_space=pltpu.SMEM),
            pl.BlockSpec((rows, lane_rows, LANES), lambda j: (0, 0, 0)),
        ],
        out_specs=pl.BlockSpec((rows, lane_rows, LANES), lambda j: (0, 0, 0)),
        out_shape=jax.ShapeDtypeStruct((rows, lane_rows, LANES), jnp.float32),
        scratch_shapes=[pltpu.VMEM((lane_rows, LANES), jnp.float32) for _ in range(rows)],
        cost_estimate=pl.CostEstimate(
            flops=4 * rows * probes * block_len * LANES,
            transcendentals=0,
            bytes_accessed=rows * probes * block_len * LANES * 8 + 8 * rows * lane_rows * LANES,
        ),
        input_output_aliases={3: 0},
    )(tok >> 7, tok & (LANES - 1), w, init)
    return out


def shards(hidden, queries, probes, counts, block_slot, key_store, stored_next_tokens, head_weight):
    rows_dev = hidden.shape[0]
    piece_cols = head_weight.shape[1]
    local_blocks = key_store.shape[0]
    block_len = key_store.shape[1]
    key_width = key_store.shape[2]
    key_count = lax.axis_size("keys")
    vocab_count = lax.axis_size("vocab")
    devices = key_count * vocab_count
    probe_cap = probes.shape[1]
    vocab_size = devices * piece_cols
    both = ("keys", "vocab")

    group_queries = lax.all_gather(queries, "keys", axis=0, tiled=True)
    flat_keys = key_store.reshape(local_blocks * block_len, key_width)
    key_norms = jnp.sum(jnp.square(flat_keys.astype(jnp.float32)), axis=1)
    query_norms = jnp.sum(jnp.square(group_queries.astype(jnp.float32)), axis=1)
    inner_prod = lax.dot_general(
        group_queries, flat_keys, (((1,), (1,)), ((), ())), preferred_element_type=jnp.float32
    )
    score_scale = 0.5 / math.sqrt(key_width)
    scores = -(query_norms[:, None] + key_norms[None, :] - 2.0 * inner_prod) * score_scale
    slot_ids = block_slot[probes]
    outgoing = scores.reshape(key_count, rows_dev, local_blocks, block_len)
    incoming = lax.all_to_all(outgoing, "keys", split_axis=0, concat_axis=2, tiled=True)
    every_slot = incoming.reshape(rows_dev, key_count * local_blocks, block_len)
    chosen = jnp.take_along_axis(every_slot, slot_ids[:, :, None], axis=1)
    live_mask = (jnp.arange(probe_cap, dtype=jnp.int32)[None, :] < counts[:, None])[:, :, None]
    best_score = jnp.max(jnp.where(live_mask, chosen, -jnp.inf), axis=(1, 2), keepdims=True)
    raised = jnp.where(live_mask, jnp.exp(chosen - best_score), 0.0)
    weights = raised / jnp.sum(raised, axis=(1, 2), keepdims=True)
    tokens = stored_next_tokens[slot_ids]
    half = probe_cap // 2
    zeros = jnp.zeros((rows_dev, vocab_size // LANES, LANES), jnp.float32)
    knn_first = knn_scatter(tokens[:, :half], weights[:, :half], zeros)
    gathered = lax.all_gather(hidden, both, axis=0, tiled=False)
    gathered, knn_first = lax.optimization_barrier((gathered, knn_first))
    logits = jnp.einsum("dri,ic->drc", gathered, head_weight, preferred_element_type=jnp.float32)
    local_peak = jnp.max(logits, axis=2, keepdims=True)
    shifted = logits - local_peak
    local_sum = jnp.sum(jnp.exp(shifted), axis=2, keepdims=True)
    spare = jnp.zeros(shifted.shape[:2] + (LANES - (piece_cols + 2) % LANES,), jnp.float32)
    payload = jnp.concatenate([shifted, local_peak, local_sum, spare], axis=2)
    payload, knn_first = lax.optimization_barrier((payload, knn_first))
    got = lax.all_to_all(payload, both, split_axis=0, concat_axis=0, tiled=True)
    knn_mass = knn_scatter(tokens[:, half:], weights[:, half:], knn_first).reshape(rows_dev, vocab_size)
    got = got.reshape(devices, rows_dev, payload.shape[2])
    piece_peak = got[:, :, piece_cols]
    row_peak = jnp.max(piece_peak, axis=0)
    row_sum = jnp.sum(got[:, :, piece_cols + 1] * jnp.exp(piece_peak - row_peak[None, :]), axis=0)
    offset = piece_peak - (row_peak + jnp.log(row_sum))[None, :]
    log_probs = got[:, :, :piece_cols] + offset[:, :, None]
    log_probs = log_probs.transpose(1, 0, 2).reshape(rows_dev, vocab_size)

    return jnp.log(
        LAMBDA * (knn_mass + SMOOTH / vocab_size) / (1.0 + SMOOTH)
        + (1.0 - LAMBDA) * jnp.exp(log_probs)
    )


def solution(mesh):
    placed = (
        P(("keys", "vocab"), None),
        P(("keys", "vocab"), None),
        P(("keys", "vocab"), None),
        P(("keys", "vocab")),
        P(),
        P("keys", None, None),
        P(),
        P(None, ("keys", "vocab")),
    )
    return jax.shard_map(
        shards, mesh=mesh, in_specs=placed, out_specs=P(("keys", "vocab"), None), check_vma=False
    )
```
